256 devices in a mesh: space: 64 (over z, x, core), head: 4 (over y).
Axes of the slice: x: 4, y: 4, z: 8, core: 2. Of those that a mesh axis runs over, the one named last changes fastest.
Arguments:
- features: bfloat16 [512, 16, 16, 128], P('space', None, None, 'head'), may hold values from -6 to 6
- mask: int32 [512, 16, 16], P('space'), may hold values from 0 to 1, as said below
- conv1_weight: bfloat16 [27, 128, 128], replicated, may hold values from -0.21875 to 0.21875
- conv2_weight: bfloat16 [27, 128, 128], replicated, may hold values from -0.21875 to 0.21875
- down_weight: bfloat16 [8, 128, 512], replicated, may hold values from -0.1875 to 0.1875
- norm_gain: float32 [512], replicated, may hold values from 0.1 to 1.9
- qkv_weight: bfloat16 [512, 3, 512], P(None, None, 'head'), may hold values from -2 to 2
- out_weight: bfloat16 [512, 512], P('head'), may hold values from -0.25 to 0.25
Outputs:
- refined: bfloat16 [512, 16, 16, 128], P('space', None, None, 'head')
- level_out: bfloat16 [16384, 512], P('space', 'head')
The draws below stay inside these ranges and needn't reach their ends.
Inputs may be any that keep to these rules, and one draw needn't show every extreme that they name: `mask`: A voxel is occupied only inside an active brick of 8^3 aligned voxels; the first brick and its first voxel are always occupied.
All inputs are finite; a program needn't handle non-finite values.
Results may differ from the reference program's by a relative error of at most 0.012.
Values may be sent and summed in bfloat16 or wider, within the bound.
No kernel may reach another device: no remote copies, remote signals or barrier semaphores. Data moves between devices by JAX's collectives and lax.ppermute only.
A program may use at most 64 MiB of HBM per device.

```python
import math
import jax
import jax.numpy as jnp
from jax import lax

C = 128
D = 512
HEADS = 8
HD = 64
BRICK = 8
VY = 16
VZ = 16
NX = 512
NT = 16384


def draw_mask(key, part):
    brick_key = jax.random.fold_in(key, 11)
    voxel_key = jax.random.fold_in(key, 12)
    bricks = jax.random.randint(brick_key, (NX // BRICK, VY // BRICK, VZ // BRICK), 0, 10) < 6
    bricks = bricks.at[0, 0, 0].set(True)
    bricks = jnp.repeat(jnp.repeat(jnp.repeat(bricks, BRICK, 0), BRICK, 1), BRICK, 2)
    voxels = jax.random.randint(voxel_key, (NX, VY, VZ), 0, 10) < 7
    voxels = voxels.at[0, 0, 0].set(True)
    return (bricks & voxels).astype(jnp.int32)


def draw_qkv_weight(key, part):
    return (jnp.clip(jax.random.normal(key, (D, 3, D), jnp.float32), -6.0, 6.0) * (2.0 / math.sqrt(D))).astype(jnp.bfloat16)


def block_scale(key, dims, cuts, low, high):
    def one(position, parts):
        steps = jax.random.uniform(jax.random.fold_in(jax.random.fold_in(key, 6), position), (parts,), jnp.float32, low / len(cuts), high / len(cuts))
        return jnp.repeat(jnp.exp(steps), dims[position] // parts).reshape((-1,) + (1,) * (len(dims) - position - 1))

    level = one(*cuts[0])
    for cut in cuts[1:]:
        level = level * one(*cut)
    return level


def normal_values(key, dims, spread, bound, split=(), dtype=jnp.bfloat16):
    drawn = jax.random.normal(key, dims, jnp.float32) * spread
    if len(split) > 0:
        drawn = block_scale(key, dims, split, -0.22, 0.18) * drawn
    return jnp.clip(drawn, min=-bound, max=bound).astype(dtype)


def setup_inputs(seed: int = 0) -> dict:
    seeds = jax.random.split(jax.random.key(seed), 9)
    return {
        "features": normal_values(seeds[0], (NX, VY, VZ, C), 1.0, 6.0, ((0, 64), (3, 4))),
        "mask": draw_mask(jax.random.fold_in(seeds[8], 71), 0),
        "conv1_weight": normal_values(seeds[2], (27, C, C), (27 * C // 4) ** -0.5, 0.21875),
        "conv2_weight": normal_values(seeds[3], (27, C, C), (27 * C // 4) ** -0.5, 0.21875),
        "down_weight": normal_values(seeds[4], (8, C, D), (8 * C) ** -0.5, 0.1875),
        "norm_gain": jnp.clip(1.0 + 0.18 * jax.random.normal(seeds[5], (D,), jnp.float32), 0.1, 1.9),
        "qkv_weight": draw_qkv_weight(jax.random.fold_in(seeds[8], 71), 0),
        "out_weight": normal_values(seeds[7], (D, D), D ** -0.5, 0.25, ((0, 4),)),
    }


def convolve(field, weight):
    padded = jnp.pad(field, ((1, 1), (1, 1), (1, 1), (0, 0)))
    total = jnp.zeros((NX * VY * VZ, C), jnp.float32)
    for offset in range(27):
        first, second, third = (offset // 9, offset // 3 % 3, offset % 3)
        slab = padded[first:first + NX, second:second + VY, third:third + VZ].reshape(-1, C)
        total = total + jnp.dot(slab, weight[offset], preferred_element_type=jnp.float32)
    return total.reshape(NX, VY, VZ, C)

def reference(features, mask, conv1_weight, conv2_weight, down_weight, norm_gain, qkv_weight, out_weight):
    occupied = mask.astype(jnp.float32)[..., None]
    masked = features * mask.astype(jnp.bfloat16)[..., None]
    pre1 = convolve(masked, conv1_weight)
    hidden = (occupied * jax.nn.silu(pre1)).astype(jnp.bfloat16)
    pre2 = convolve(hidden, conv2_weight)
    refined = (occupied * (features.astype(jnp.float32) + pre2)).astype(jnp.bfloat16)
    cells = refined.reshape(NX // 2, 2, VY // 2, 2, VZ // 2, 2, C).transpose(0, 2, 4, 1, 3, 5, 6).reshape(NT, 8 * C)
    coarse = jnp.dot(cells, down_weight.reshape(8 * C, D), preferred_element_type=jnp.float32).astype(jnp.bfloat16)
    live = mask.reshape(NX // 2, 2, VY // 2, 2, VZ // 2, 2).max(axis=(1, 3, 5)).reshape(-1) > 0
    wide = coarse.astype(jnp.float32)
    normed = (wide * lax.rsqrt(lax.optimization_barrier(jnp.mean(wide * wide, axis=1, keepdims=True)) + 1e-05) * norm_gain).astype(jnp.bfloat16)
    proj = jnp.dot(normed, qkv_weight.reshape(D, 3 * D), preferred_element_type=jnp.float32).astype(jnp.bfloat16)
    proj = proj.reshape(NT, 3, HEADS, HD).astype(jnp.float32)
    query, keys, values = (proj[:, 0], proj[:, 1], proj[:, 2])
    scale = HD ** (-0.5)
    block = math.gcd(NT, 256)

    def attend(query_block):
        scores = jnp.einsum('qhd,khd->hqk', query_block, keys) * scale
        scores = jnp.where(live[None, None, :], scores, -1e+30)
        top = lax.optimization_barrier(jnp.max(scores, axis=-1, keepdims=True))
        expo = jnp.where(live[None, None, :], jnp.exp(scores - top), 0.0)
        sums = lax.optimization_barrier(jnp.sum(expo, axis=-1))
        rounded = lax.optimization_barrier(expo.astype(jnp.bfloat16)).astype(jnp.float32)
        numer = jnp.einsum('hqk,khd->qhd', rounded, values)
        return (numer / jnp.transpose(sums)[..., None]).reshape(block, D)
    attn = lax.map(attend, query.reshape(NT // block, block, HEADS, HD)).reshape(NT, D).astype(jnp.bfloat16)
    level_out = (wide + jnp.dot(attn, out_weight, preferred_element_type=jnp.float32)).astype(jnp.bfloat16)
    return (refined, level_out)
```

```python
import jax
import jax.numpy as jnp
from jax import lax
from jax.sharding import PartitionSpec as P

HEADS = 8
KEY_BLOCK = 1024


def with_halo(cells, axis, width):
    count = lax.axis_size(axis)
    ends = count - 1
    head = lax.slice_in_dim(cells, 0, width, axis=0)
    tail = lax.slice_in_dim(cells, cells.shape[0] - width, cells.shape[0], axis=0)
    return jnp.concatenate(
        [
            lax.ppermute(tail, axis, [(i, i + 1) for i in range(ends)]),
            cells,
            lax.ppermute(head, axis, [(i + 1, i) for i in range(ends)]),
        ],
        axis=0,
    )


def convolve(rimmed, weight):
    chans = weight.shape[1]
    kernel = weight.reshape(3, 3, 3, chans, weight.shape[2])
    out = lax.conv_general_dilated(
        rimmed[None],
        kernel,
        window_strides=(1, 1, 1),
        padding=((0, 0), (1, 1), (1, 1)),
        dimension_numbers=("NDHWC", "DHWIO", "NDHWC"),
        preferred_element_type=jnp.float32,
    )
    return out[0]


def to_cells(field):
    nx, ny, nz, count = field.shape
    blocks = field.reshape(nx // 2, 2, ny // 2, 2, nz // 2, 2, count).transpose(0, 2, 4, 1, 3, 5, 6)
    return blocks.reshape(nx // 2 * (ny // 2) * (nz // 2), 8 * count)


def body(
    features, mask, conv1_weight, conv2_weight, down_weight, norm_gain, qkv_weight, out_weight
):
    member = lax.axis_index("head")
    nx, ny, nz, local = features.shape
    width = down_weight.shape[2]
    chans = conv1_weight.shape[1]
    tokens = nx // 2 * (ny // 2) * (nz // 2)
    occupied = mask.astype(jnp.float32)[..., None]
    masked = features * mask.astype(jnp.bfloat16)[..., None]
    rimmed = lax.all_gather(with_halo(masked, "space", 1), "head", axis=3, tiled=True)
    whole_masked = lax.slice_in_dim(rimmed, 1, nx + 1, axis=0)
    pre1 = convolve(rimmed, conv1_weight)
    hidden = (occupied * jax.nn.silu(pre1)).astype(jnp.bfloat16)
    pre2 = convolve(with_halo(hidden, "space", 1), conv2_weight)
    refined_all = (occupied * (whole_masked.astype(jnp.float32) + pre2)).astype(jnp.bfloat16)
    refined = lax.dynamic_slice_in_dim(refined_all, member * local, local, 3)
    coarse = jnp.dot(
        to_cells(refined_all),
        down_weight.reshape(8 * chans, width),
        preferred_element_type=jnp.float32,
    ).astype(jnp.bfloat16)
    wide = coarse.astype(jnp.float32)
    normed = (
        wide * lax.rsqrt(jnp.mean(wide * wide, axis=1, keepdims=True) + 1e-05) * norm_gain
    ).astype(jnp.bfloat16)
    local_cols = qkv_weight.shape[2]
    proj = jnp.dot(
        normed, qkv_weight.reshape(width, 3 * local_cols), preferred_element_type=jnp.float32
    )
    proj = proj.astype(jnp.bfloat16).reshape(tokens, 3, local_cols)
    head_size = width // HEADS
    heads_here = local_cols // head_size
    query = proj[:, 0].reshape(tokens, heads_here, head_size)
    live_cell = (
        mask.reshape(nx // 2, 2, ny // 2, 2, nz // 2, 2)
        .max(axis=(1, 3, 5))
        .reshape(1, -1)
        .astype(jnp.bfloat16)
    )
    span = 2 * local_cols
    live_len = -(-tokens // span) * span
    live_rows = jnp.pad(live_cell, ((0, 0), (0, live_len - tokens))).reshape(-1, span)
    live_count = live_rows.shape[0]
    live_rows = jnp.pad(live_rows, ((0, -(-live_count // 8) * 8 - live_count), (0, 0)))
    piece = jnp.concatenate([proj[:, 1], proj[:, 2]], axis=1)
    piece = jnp.concatenate([piece, live_rows], axis=0)
    rows = piece.shape[0]
    gathered = lax.all_gather(piece[None], "space", axis=0, tiled=True)
    parts = gathered.shape[0]
    count = parts * tokens
    piece_keys = gathered[:, :tokens, :local_cols].reshape(count, heads_here, head_size)
    piece_values = gathered[:, :tokens, local_cols:].reshape(count, heads_here, head_size)
    piece_live = gathered[:, tokens : tokens + live_count].reshape(parts, -1)[:, :tokens].reshape(count)
    bias = jnp.where(piece_live > 0, 0.0, -1e30).astype(jnp.float32)
    scale = head_size ** (-0.5)

    def one_block(carry, block):
        top_old, sums, accum = carry
        block_keys, block_values, block_bias = block
        scores = (
            jnp.einsum("qhd,khd->hqk", query, block_keys, preferred_element_type=jnp.float32)
            * scale
            + block_bias[None, None, :]
        )
        top_new = jnp.maximum(top_old, jnp.max(scores, axis=-1))
        expo = jnp.exp(scores - top_new[..., None])
        factor = jnp.exp(top_old - top_new)
        sums = sums * factor + jnp.sum(expo, axis=-1)
        accum = accum * factor[..., None] + jnp.einsum(
            "hqk,khd->hqd",
            expo.astype(jnp.bfloat16),
            block_values,
            preferred_element_type=jnp.float32,
        )
        return ((top_new, sums, accum), None)

    start_state = (
        jnp.full((heads_here, tokens), -1e30, jnp.float32),
        jnp.zeros((heads_here, tokens), jnp.float32),
        jnp.zeros((heads_here, tokens, head_size), jnp.float32),
    )
    size = KEY_BLOCK if count % KEY_BLOCK == 0 else tokens
    blocks = count // size
    stacked = (
        piece_keys.reshape(blocks, size, heads_here, head_size),
        piece_values.reshape(blocks, size, heads_here, head_size),
        bias.reshape(blocks, size),
    )
    carry, unused = lax.scan(one_block, start_state, stacked)
    top_final, sums, accum = carry
    attn = (
        (accum / sums[..., None])
        .transpose(1, 0, 2)
        .reshape(tokens, local_cols)
        .astype(jnp.bfloat16)
    )
    cols_w = lax.all_to_all(out_weight, "head", 1, 0, tiled=True)
    attn_all = lax.all_gather(attn, "head", axis=1, tiled=True)
    mixed = jnp.dot(attn_all, cols_w, preferred_element_type=jnp.float32)
    mine = lax.dynamic_slice_in_dim(wide, member * local_cols, local_cols, 1)
    level_out = (mine + mixed).astype(jnp.bfloat16)
    return (refined, level_out)


def solution(mesh):
    in_specs = (
        P("space", None, None, "head"),
        P("space", None, None),
        P(),
        P(),
        P(),
        P(),
        P(None, None, "head"),
        P("head", None),
    )
    out_specs = (P("space", None, None, "head"), P("space", "head"))
    return jax.shard_map(body, mesh=mesh, in_specs=in_specs, out_specs=out_specs, check_vma=False)
```

```python
import jax
import jax.numpy as jnp
from jax import lax
from jax.experimental import pallas as pl
from jax.experimental.pallas import tpu as pltpu
from jax.sharding import PartitionSpec as P

HEADS = 8
CHUNKS_PER_STEP = 8


def gather_head(piece_for):
    count = lax.axis_size("head")
    member = lax.axis_index("head")
    got = [piece_for(0)]
    for shift in range(1, count):
        got.append(
            lax.ppermute(
                piece_for(shift), "head", [(i, (i + shift) % count) for i in range(count)]
            )
        )
    ring = jnp.stack([got[0]] + [got[count - t] for t in range(1, count)])
    twice = jnp.concatenate([ring, ring], axis=0)
    return lax.dynamic_slice_in_dim(twice, (count - member) % count, count, axis=0)


def attend_kernel(q_ref, kv_ref, o_ref, top_ref, sum_ref, acc_ref, *, tokens, cols, hd, scale):
    step = pl.program_id(0)
    heads = cols // hd

    @pl.when(step == 0)
    def _():
        top_ref[...] = jnp.full(top_ref.shape, -1e30, jnp.float32)
        sum_ref[...] = jnp.zeros(sum_ref.shape, jnp.float32)
        acc_ref[...] = jnp.zeros(acc_ref.shape, jnp.float32)

    q = q_ref[...]
    lanes = lax.broadcasted_iota(jnp.int32, q.shape, 1) // hd
    query = jnp.concatenate([jnp.where(lanes == h, q, jnp.zeros_like(q)) for h in range(heads)], 0)
    for chunk in range(kv_ref.shape[0]):
        keys = kv_ref[chunk, :tokens, :cols]
        values = kv_ref[chunk, :tokens, cols:]
        live = kv_ref[chunk, tokens : tokens + 1, :tokens]
        bias = jnp.where(live > 0, 0.0, -1e30).astype(jnp.float32)
        scores = (
            lax.dot_general(
                query, keys, (((1,), (1,)), ((), ())), preferred_element_type=jnp.float32
            )
            * scale
            + bias
        )
        top_old = top_ref[...]
        top_new = jnp.maximum(top_old, jnp.max(scores, axis=-1, keepdims=True))
        expo = jnp.exp(scores - top_new)
        factor = jnp.exp(top_old - top_new)
        sum_ref[...] = sum_ref[...] * factor + jnp.sum(expo, axis=-1, keepdims=True)
        acc_ref[...] = acc_ref[...] * factor + jnp.dot(
            expo.astype(jnp.bfloat16), values, preferred_element_type=jnp.float32
        )
        top_ref[...] = top_new

    @pl.when(step == pl.num_programs(0) - 1)
    def _():
        ratio = acc_ref[...] / sum_ref[...]
        out = jnp.zeros(q.shape, jnp.float32)
        for h in range(heads):
            out = jnp.where(lanes == h, ratio[h * tokens : (h + 1) * tokens], out)
        o_ref[...] = out.astype(o_ref.dtype)


def attend(query, gathered, tokens, cols, hd, scale):
    parts, rows, span = gathered.shape
    qrows = query.shape[0] * (cols // hd)
    per = CHUNKS_PER_STEP if parts % CHUNKS_PER_STEP == 0 else 1
    kernel = lambda *refs: attend_kernel(*refs, tokens=tokens, cols=cols, hd=hd, scale=scale)
    return pl.pallas_call(
        kernel,
        grid=(parts // per,),
        in_specs=[
            pl.BlockSpec(query.shape, lambda i: (0, 0)),
            pl.BlockSpec((per, rows, span), lambda i: (i, 0, 0)),
        ],
        out_specs=pl.BlockSpec(query.shape, lambda i: (0, 0)),
        out_shape=jax.ShapeDtypeStruct(query.shape, jnp.bfloat16),
        scratch_shapes=[
            pltpu.VMEM((qrows, 1), jnp.float32),
            pltpu.VMEM((qrows, 1), jnp.float32),
            pltpu.VMEM((qrows, span - cols), jnp.float32),
        ],
    )(query, gathered)


def with_halo(cells, axis, width):
    count = lax.axis_size(axis)
    ends = count - 1
    head = lax.slice_in_dim(cells, 0, width, axis=0)
    tail = lax.slice_in_dim(cells, cells.shape[0] - width, cells.shape[0], axis=0)
    return jnp.concatenate(
        [
            lax.ppermute(tail, axis, [(i, i + 1) for i in range(ends)]),
            cells,
            lax.ppermute(head, axis, [(i + 1, i) for i in range(ends)]),
        ],
        axis=0,
    )


def convolve(rimmed, weight):
    chans = weight.shape[1]
    kernel = weight.reshape(3, 3, 3, chans, weight.shape[2])
    out = lax.conv_general_dilated(
        rimmed[None],
        kernel,
        window_strides=(1, 1, 1),
        padding=((0, 0), (1, 1), (1, 1)),
        dimension_numbers=("NDHWC", "DHWIO", "NDHWC"),
        preferred_element_type=jnp.float32,
    )
    return out[0]


def to_cells(field):
    nx, ny, nz, count = field.shape
    blocks = field.reshape(nx // 2, 2, ny // 2, 2, nz // 2, 2, count).transpose(0, 2, 4, 1, 3, 5, 6)
    return blocks.reshape(nx // 2 * (ny // 2) * (nz // 2), 8 * count)


def body(
    features, mask, conv1_weight, conv2_weight, down_weight, norm_gain, qkv_weight, out_weight
):
    member = lax.axis_index("head")
    nx, ny, nz, local = features.shape
    width = down_weight.shape[2]
    chans = conv1_weight.shape[1]
    tokens = nx // 2 * (ny // 2) * (nz // 2)
    occupied = mask.astype(jnp.float32)[..., None]
    masked = features * mask.astype(jnp.bfloat16)[..., None]
    halo = with_halo(masked, "space", 1)
    rimmed = gather_head(lambda shift: halo)
    rimmed = jnp.moveaxis(rimmed, 0, 3).reshape(halo.shape[:3] + (-1,))
    whole_masked = lax.slice_in_dim(rimmed, 1, nx + 1, axis=0)
    pre1 = convolve(rimmed, conv1_weight)
    hidden = (occupied * jax.nn.silu(pre1)).astype(jnp.bfloat16)
    pre2 = convolve(with_halo(hidden, "space", 1), conv2_weight)
    refined_all = (occupied * (whole_masked.astype(jnp.float32) + pre2)).astype(jnp.bfloat16)
    refined = lax.dynamic_slice_in_dim(refined_all, member * local, local, 3)
    coarse = jnp.dot(
        to_cells(refined_all),
        down_weight.reshape(8 * chans, width),
        preferred_element_type=jnp.float32,
    ).astype(jnp.bfloat16)
    wide = coarse.astype(jnp.float32)
    normed = (
        wide * lax.rsqrt(jnp.mean(wide * wide, axis=1, keepdims=True) + 1e-05) * norm_gain
    ).astype(jnp.bfloat16)
    local_cols = qkv_weight.shape[2]
    proj = jnp.dot(
        normed, qkv_weight.reshape(width, 3 * local_cols), preferred_element_type=jnp.float32
    )
    proj = proj.astype(jnp.bfloat16).reshape(tokens, 3, local_cols)
    head_size = width // HEADS
    heads_here = local_cols // head_size
    query = proj[:, 0]
    live_cell = (
        mask.reshape(nx // 2, 2, ny // 2, 2, nz // 2, 2)
        .max(axis=(1, 3, 5))
        .reshape(1, -1)
        .astype(jnp.bfloat16)
    )
    span = 2 * local_cols
    live_rows = jnp.pad(live_cell, ((0, 0), (0, span - tokens)))
    live_rows = jnp.pad(live_rows, ((0, 15), (0, 0)))
    piece = jnp.concatenate([proj[:, 1], proj[:, 2]], axis=1)
    piece = jnp.concatenate([piece, live_rows], axis=0)
    gathered = lax.all_gather(piece[None], "space", axis=0, tiled=True)
    scale = head_size ** (-0.5)
    attn = attend(query, gathered, tokens, local_cols, head_size, scale)
    cols_w = gather_head(
        lambda shift: lax.dynamic_slice_in_dim(
            out_weight, (member + shift) % lax.axis_size("head") * local_cols, local_cols, 1
        )
    ).reshape(width, local_cols)
    attn_all = jnp.moveaxis(gather_head(lambda shift: attn), 0, 1).reshape(tokens, width)
    mixed = jnp.dot(attn_all, cols_w, preferred_element_type=jnp.float32)
    mine = lax.dynamic_slice_in_dim(wide, member * local_cols, local_cols, 1)
    level_out = (mine + mixed).astype(jnp.bfloat16)
    return (refined, level_out)


def solution(mesh):
    in_specs = (
        P("space", None, None, "head"),
        P("space", None, None),
        P(),
        P(),
        P(),
        P(),
        P(None, None, "head"),
        P("head", None),
    )
    out_specs = (P("space", None, None, "head"), P("space", "head"))
    return jax.shard_map(body, mesh=mesh, in_specs=in_specs, out_specs=out_specs, check_vma=False)
```

```python
import jax
import jax.numpy as jnp
from jax import lax
from jax.experimental import pallas as pl
from jax.experimental.pallas import tpu as pltpu
from jax.sharding import PartitionSpec as P

HEADS = 8
CHUNKS_PER_STEP = 8


def gather_head(piece_for):
    count = lax.axis_size("head")
    member = lax.axis_index("head")
    got = [piece_for(0)]
    for shift in range(1, count):
        got.append(
            lax.ppermute(
                piece_for(shift), "head", [(i, (i + shift) % count) for i in range(count)]
            )
        )
    ring = jnp.stack([got[0]] + [got[count - t] for t in range(1, count)])
    twice = jnp.concatenate([ring, ring], axis=0)
    return lax.dynamic_slice_in_dim(twice, (count - member) % count, count, axis=0)


def attend_kernel(q_ref, kv_ref, top_in, sum_in, acc_in, *rest, keys_per, cols, hd, scale, final):
    if final:
        o_ref, top_ref, sum_ref, acc_ref = rest
    else:
        top_ref, sum_ref, acc_ref = rest
    step = pl.program_id(0)
    heads = cols // hd
    qt = q_ref.shape[0]

    @pl.when(step == 0)
    def _():
        top_ref[...] = top_in[...]
        sum_ref[...] = sum_in[...]
        acc_ref[...] = acc_in[...]

    q = q_ref[...]
    lanes = lax.broadcasted_iota(jnp.int32, q.shape, 1) // hd
    query = jnp.concatenate([jnp.where(lanes == h, q, jnp.zeros_like(q)) for h in range(heads)], 0)
    for chunk in range(kv_ref.shape[0]):
        keys = kv_ref[chunk, :keys_per, :cols]
        values = kv_ref[chunk, :keys_per, cols:]
        live = kv_ref[chunk, keys_per : keys_per + 1, :keys_per]
        bias = jnp.where(live > 0, 0.0, -1e30).astype(jnp.float32)
        scores = (
            lax.dot_general(
                query, keys, (((1,), (1,)), ((), ())), preferred_element_type=jnp.float32
            )
            * scale
            + bias
        )
        top_old = top_ref[...]
        top_new = jnp.maximum(top_old, jnp.max(scores, axis=-1, keepdims=True))
        expo = jnp.exp(scores - top_new)
        factor = jnp.exp(top_old - top_new)
        sum_ref[...] = sum_ref[...] * factor + jnp.sum(expo, axis=-1, keepdims=True)
        acc_ref[...] = acc_ref[...] * factor + jnp.dot(
            expo.astype(jnp.bfloat16), values, preferred_element_type=jnp.float32
        )
        top_ref[...] = top_new

    if final:

        @pl.when(step == pl.num_programs(0) - 1)
        def _():
            ratio = acc_ref[...] / sum_ref[...]
            out = jnp.zeros(q.shape, jnp.float32)
            for h in range(heads):
                out = jnp.where(lanes == h, ratio[h * qt : (h + 1) * qt], out)
            o_ref[...] = out.astype(o_ref.dtype)


def attend(query, gathered, state, keys_per, cols, hd, scale, final):
    parts, rows, span = gathered.shape
    qrows = query.shape[0] * (cols // hd)
    per = CHUNKS_PER_STEP if parts % CHUNKS_PER_STEP == 0 else 1
    kernel = lambda *refs: attend_kernel(
        *refs, keys_per=keys_per, cols=cols, hd=hd, scale=scale, final=final
    )
    shapes = [(qrows, 1), (qrows, 1), (qrows, span - cols)]
    fixed = lambda i: (0, 0)
    state_specs = [pl.BlockSpec(shape, fixed) for shape in shapes]
    if final:
        out_specs = pl.BlockSpec(query.shape, fixed)
        out_shape = jax.ShapeDtypeStruct(query.shape, jnp.bfloat16)
        scratch = [pltpu.VMEM(shape, jnp.float32) for shape in shapes]
    else:
        out_specs = state_specs
        out_shape = [jax.ShapeDtypeStruct(shape, jnp.float32) for shape in shapes]
        scratch = []
    return pl.pallas_call(
        kernel,
        grid=(parts // per,),
        in_specs=[pl.BlockSpec(query.shape, fixed), pl.BlockSpec((per, rows, span), lambda i: (i, 0, 0))]
        + state_specs,
        out_specs=out_specs,
        out_shape=out_shape,
        scratch_shapes=scratch,
    )(query, gathered, *state)


def with_halo(cells, axis, width):
    count = lax.axis_size(axis)
    ends = count - 1
    head = lax.slice_in_dim(cells, 0, width, axis=0)
    tail = lax.slice_in_dim(cells, cells.shape[0] - width, cells.shape[0], axis=0)
    return jnp.concatenate(
        [
            lax.ppermute(tail, axis, [(i, i + 1) for i in range(ends)]),
            cells,
            lax.ppermute(head, axis, [(i + 1, i) for i in range(ends)]),
        ],
        axis=0,
    )


def convolve(rimmed, weight):
    chans = weight.shape[1]
    kernel = weight.reshape(3, 3, 3, chans, weight.shape[2])
    out = lax.conv_general_dilated(
        rimmed[None],
        kernel,
        window_strides=(1, 1, 1),
        padding=((0, 0), (1, 1), (1, 1)),
        dimension_numbers=("NDHWC", "DHWIO", "NDHWC"),
        preferred_element_type=jnp.float32,
    )
    return out[0]


def to_cells(field):
    nx, ny, nz, count = field.shape
    blocks = field.reshape(nx // 2, 2, ny // 2, 2, nz // 2, 2, count).transpose(0, 2, 4, 1, 3, 5, 6)
    return blocks.reshape(nx // 2 * (ny // 2) * (nz // 2), 8 * count)


def body(
    features, mask, conv1_weight, conv2_weight, down_weight, norm_gain, qkv_weight, out_weight
):
    member = lax.axis_index("head")
    nx, ny, nz, local = features.shape
    width = down_weight.shape[2]
    chans = conv1_weight.shape[1]
    tokens = nx // 2 * (ny // 2) * (nz // 2)
    occupied = mask.astype(jnp.float32)[..., None]
    masked = features * mask.astype(jnp.bfloat16)[..., None]
    halo = with_halo(masked, "space", 1)
    rimmed = gather_head(lambda shift: halo)
    rimmed = jnp.moveaxis(rimmed, 0, 3).reshape(halo.shape[:3] + (-1,))
    whole_masked = lax.slice_in_dim(rimmed, 1, nx + 1, axis=0)
    pre1 = convolve(rimmed, conv1_weight)
    hidden = (occupied * jax.nn.silu(pre1)).astype(jnp.bfloat16)
    pre2 = convolve(with_halo(hidden, "space", 1), conv2_weight)
    refined_all = (occupied * (whole_masked.astype(jnp.float32) + pre2)).astype(jnp.bfloat16)
    refined = lax.dynamic_slice_in_dim(refined_all, member * local, local, 3)
    coarse = jnp.dot(
        to_cells(refined_all),
        down_weight.reshape(8 * chans, width),
        preferred_element_type=jnp.float32,
    ).astype(jnp.bfloat16)
    wide = coarse.astype(jnp.float32)
    normed = (
        wide * lax.rsqrt(jnp.mean(wide * wide, axis=1, keepdims=True) + 1e-05) * norm_gain
    ).astype(jnp.bfloat16)
    local_cols = qkv_weight.shape[2]
    proj = jnp.dot(
        normed, qkv_weight.reshape(width, 3 * local_cols), preferred_element_type=jnp.float32
    )
    proj = proj.astype(jnp.bfloat16).reshape(tokens, 3, local_cols)
    head_size = width // HEADS
    heads_here = local_cols // head_size
    query = proj[:, 0]
    live_cell = (
        mask.reshape(nx // 2, 2, ny // 2, 2, nz // 2, 2)
        .max(axis=(1, 3, 5))
        .reshape(1, -1)
        .astype(jnp.bfloat16)
    )
    span = 2 * local_cols
    half = tokens // 2
    kv = jnp.concatenate([proj[:, 1], proj[:, 2]], axis=1)
    halves = []
    for part in range(2):
        live_rows = jnp.pad(live_cell[:, part * half : (part + 1) * half], ((0, 15), (0, span - half)))
        piece = jnp.concatenate([kv[part * half : (part + 1) * half], live_rows], axis=0)
        halves.append(lax.all_gather(piece[None], "space", axis=0, tiled=True))
    scale = head_size ** (-0.5)
    qrows = tokens * heads_here
    state = (
        jnp.full((qrows, 1), -1e30, jnp.float32),
        jnp.zeros((qrows, 1), jnp.float32),
        jnp.zeros((qrows, local_cols), jnp.float32),
    )
    state = attend(query, halves[0], state, half, local_cols, head_size, scale, False)
    attn = attend(query, halves[1], state, half, local_cols, head_size, scale, True)
    cols_w = gather_head(
        lambda shift: lax.dynamic_slice_in_dim(
            out_weight, (member + shift) % lax.axis_size("head") * local_cols, local_cols, 1
        )
    ).reshape(width, local_cols)
    attn_all = jnp.moveaxis(gather_head(lambda shift: attn), 0, 1).reshape(tokens, width)
    mixed = jnp.dot(attn_all, cols_w, preferred_element_type=jnp.float32)
    mine = lax.dynamic_slice_in_dim(wide, member * local_cols, local_cols, 1)
    level_out = (mine + mixed).astype(jnp.bfloat16)
    return (refined, level_out)


def solution(mesh):
    in_specs = (
        P("space", None, None, "head"),
        P("space", None, None),
        P(),
        P(),
        P(),
        P(),
        P(None, None, "head"),
        P("head", None),
    )
    out_specs = (P("space", None, None, "head"), P("space", "head"))
    return jax.shard_map(body, mesh=mesh, in_specs=in_specs, out_specs=out_specs, check_vma=False)
```

```python
import jax
import jax.numpy as jnp
from jax import lax
from jax.experimental import pallas as pl
from jax.experimental.pallas import tpu as pltpu
from jax.sharding import PartitionSpec as P

HEADS = 8
CHUNKS_PER_STEP = 8
GROUP = 4


def gather_head(piece_for):
    count = lax.axis_size("head")
    member = lax.axis_index("head")
    got = [piece_for(0)]
    for shift in range(1, count):
        got.append(
            lax.ppermute(
                piece_for(shift), "head", [(i, (i + shift) % count) for i in range(count)]
            )
        )
    ring = jnp.stack([got[0]] + [got[count - t] for t in range(1, count)])
    twice = jnp.concatenate([ring, ring], axis=0)
    return lax.dynamic_slice_in_dim(twice, (count - member) % count, count, axis=0)


def attend_kernel(q_ref, kv_ref, o_ref, top_ref, sum_ref, acc_ref, *, tokens, cols, hd, scale):
    step = pl.program_id(0)
    heads = cols // hd

    @pl.when(step == 0)
    def _():
        top_ref[...] = jnp.full(top_ref.shape, -1e30, jnp.float32)
        sum_ref[...] = jnp.zeros(sum_ref.shape, jnp.float32)
        acc_ref[...] = jnp.zeros(acc_ref.shape, jnp.float32)

    q = q_ref[...]
    lanes = lax.broadcasted_iota(jnp.int32, q.shape, 1) // hd
    query = jnp.concatenate([jnp.where(lanes == h, q, jnp.zeros_like(q)) for h in range(heads)], 0)
    group = GROUP if kv_ref.shape[0] % GROUP == 0 else 1
    for first in range(0, kv_ref.shape[0], group):
        scores, values = [], []
        for chunk in range(first, first + group):
            keys = kv_ref[chunk, :tokens, :cols]
            values.append(kv_ref[chunk, :tokens, cols:])
            live = kv_ref[chunk, tokens : tokens + 1, :tokens]
            bias = jnp.where(live > 0, 0.0, -1e30).astype(jnp.float32)
            scores.append(
                lax.dot_general(
                    query, keys, (((1,), (1,)), ((), ())), preferred_element_type=jnp.float32
                )
                * scale
                + bias
            )
        top_old = top_ref[...]
        top_new = top_old
        for block in scores:
            top_new = jnp.maximum(top_new, jnp.max(block, axis=-1, keepdims=True))
        factor = jnp.exp(top_old - top_new)
        total = sum_ref[...] * factor
        accum = acc_ref[...] * factor
        for block, value in zip(scores, values):
            expo = jnp.exp(block - top_new)
            total = total + jnp.sum(expo, axis=-1, keepdims=True)
            accum = accum + jnp.dot(
                expo.astype(jnp.bfloat16), value, preferred_element_type=jnp.float32
            )
        sum_ref[...] = total
        acc_ref[...] = accum
        top_ref[...] = top_new

    @pl.when(step == pl.num_programs(0) - 1)
    def _():
        ratio = acc_ref[...] / sum_ref[...]
        out = jnp.zeros(q.shape, jnp.float32)
        for h in range(heads):
            out = jnp.where(lanes == h, ratio[h * tokens : (h + 1) * tokens], out)
        o_ref[...] = out.astype(o_ref.dtype)


def attend(query, gathered, tokens, cols, hd, scale):
    parts, rows, span = gathered.shape
    qrows = query.shape[0] * (cols // hd)
    per = CHUNKS_PER_STEP if parts % CHUNKS_PER_STEP == 0 else 1
    kernel = lambda *refs: attend_kernel(*refs, tokens=tokens, cols=cols, hd=hd, scale=scale)
    return pl.pallas_call(
        kernel,
        grid=(parts // per,),
        in_specs=[
            pl.BlockSpec(query.shape, lambda i: (0, 0)),
            pl.BlockSpec((per, rows, span), lambda i: (i, 0, 0)),
        ],
        out_specs=pl.BlockSpec(query.shape, lambda i: (0, 0)),
        out_shape=jax.ShapeDtypeStruct(query.shape, jnp.bfloat16),
        scratch_shapes=[
            pltpu.VMEM((qrows, 1), jnp.float32),
            pltpu.VMEM((qrows, 1), jnp.float32),
            pltpu.VMEM((qrows, span - cols), jnp.float32),
        ],
    )(query, gathered)


def with_halo(cells, axis, width):
    count = lax.axis_size(axis)
    ends = count - 1
    head = lax.slice_in_dim(cells, 0, width, axis=0)
    tail = lax.slice_in_dim(cells, cells.shape[0] - width, cells.shape[0], axis=0)
    return jnp.concatenate(
        [
            lax.ppermute(tail, axis, [(i, i + 1) for i in range(ends)]),
            cells,
            lax.ppermute(head, axis, [(i + 1, i) for i in range(ends)]),
        ],
        axis=0,
    )


def convolve(rimmed, weight):
    chans = weight.shape[1]
    kernel = weight.reshape(3, 3, 3, chans, weight.shape[2])
    out = lax.conv_general_dilated(
        rimmed[None],
        kernel,
        window_strides=(1, 1, 1),
        padding=((0, 0), (1, 1), (1, 1)),
        dimension_numbers=("NDHWC", "DHWIO", "NDHWC"),
        preferred_element_type=jnp.float32,
    )
    return out[0]


def to_cells(field):
    nx, ny, nz, count = field.shape
    blocks = field.reshape(nx // 2, 2, ny // 2, 2, nz // 2, 2, count).transpose(0, 2, 4, 1, 3, 5, 6)
    return blocks.reshape(nx // 2 * (ny // 2) * (nz // 2), 8 * count)


def body(
    features, mask, conv1_weight, conv2_weight, down_weight, norm_gain, qkv_weight, out_weight
):
    member = lax.axis_index("head")
    nx, ny, nz, local = features.shape
    width = down_weight.shape[2]
    chans = conv1_weight.shape[1]
    tokens = nx // 2 * (ny // 2) * (nz // 2)
    occupied = mask.astype(jnp.float32)[..., None]
    masked = features * mask.astype(jnp.bfloat16)[..., None]
    halo = with_halo(masked, "space", 1)
    rimmed = gather_head(lambda shift: halo)
    rimmed = jnp.moveaxis(rimmed, 0, 3).reshape(halo.shape[:3] + (-1,))
    whole_masked = lax.slice_in_dim(rimmed, 1, nx + 1, axis=0)
    pre1 = convolve(rimmed, conv1_weight)
    hidden = (occupied * jax.nn.silu(pre1)).astype(jnp.bfloat16)
    pre2 = convolve(with_halo(hidden, "space", 1), conv2_weight)
    refined_all = (occupied * (whole_masked.astype(jnp.float32) + pre2)).astype(jnp.bfloat16)
    refined = lax.dynamic_slice_in_dim(refined_all, member * local, local, 3)
    coarse = jnp.dot(
        to_cells(refined_all),
        down_weight.reshape(8 * chans, width),
        preferred_element_type=jnp.float32,
    ).astype(jnp.bfloat16)
    wide = coarse.astype(jnp.float32)
    normed = (
        wide * lax.rsqrt(jnp.mean(wide * wide, axis=1, keepdims=True) + 1e-05) * norm_gain
    ).astype(jnp.bfloat16)
    local_cols = qkv_weight.shape[2]
    proj = jnp.dot(
        normed, qkv_weight.reshape(width, 3 * local_cols), preferred_element_type=jnp.float32
    )
    proj = proj.astype(jnp.bfloat16).reshape(tokens, 3, local_cols)
    head_size = width // HEADS
    heads_here = local_cols // head_size
    query = proj[:, 0]
    live_cell = (
        mask.reshape(nx // 2, 2, ny // 2, 2, nz // 2, 2)
        .max(axis=(1, 3, 5))
        .reshape(1, -1)
        .astype(jnp.bfloat16)
    )
    span = 2 * local_cols
    live_rows = jnp.pad(live_cell, ((0, 0), (0, span - tokens)))
    live_rows = jnp.pad(live_rows, ((0, 15), (0, 0)))
    piece = jnp.concatenate([proj[:, 1], proj[:, 2]], axis=1)
    piece = jnp.concatenate([piece, live_rows], axis=0)
    gathered = lax.all_gather(piece[None], "space", axis=0, tiled=True)
    scale = head_size ** (-0.5)
    attn = attend(query, gathered, tokens, local_cols, head_size, scale)
    cols_w = gather_head(
        lambda shift: lax.dynamic_slice_in_dim(
            out_weight, (member + shift) % lax.axis_size("head") * local_cols, local_cols, 1
        )
    ).reshape(width, local_cols)
    attn_all = jnp.moveaxis(gather_head(lambda shift: attn), 0, 1).reshape(tokens, width)
    mixed = jnp.dot(attn_all, cols_w, preferred_element_type=jnp.float32)
    mine = lax.dynamic_slice_in_dim(wide, member * local_cols, local_cols, 1)
    level_out = (mine + mixed).astype(jnp.bfloat16)
    return (refined, level_out)


def solution(mesh):
    in_specs = (
        P("space", None, None, "head"),
        P("space", None, None),
        P(),
        P(),
        P(),
        P(),
        P(None, None, "head"),
        P("head", None),
    )
    out_specs = (P("space", None, None, "head"), P("space", "head"))
    return jax.shard_map(body, mesh=mesh, in_specs=in_specs, out_specs=out_specs, check_vma=False)
```

```python
import jax
import jax.numpy as jnp
from jax import lax
from jax.experimental import pallas as pl
from jax.experimental.pallas import tpu as pltpu
from jax.sharding import PartitionSpec as P

HEADS = 8
SPACE = ("chip", "core")
CHUNKS_PER_STEP = 8
GROUP = 4


def gather_head(piece_for):
    count = lax.axis_size("head")
    member = lax.axis_index("head")
    got = [piece_for(0)]
    for shift in range(1, count):
        got.append(
            lax.ppermute(
                piece_for(shift), "head", [(i, (i + shift) % count) for i in range(count)]
            )
        )
    ring = jnp.stack([got[0]] + [got[count - t] for t in range(1, count)])
    twice = jnp.concatenate([ring, ring], axis=0)
    return lax.dynamic_slice_in_dim(twice, (count - member) % count, count, axis=0)


def attend_kernel(q_ref, kv_ref, o_ref, top_ref, sum_ref, acc_ref, *, tokens, cols, hd, scale, sub):
    step = pl.program_id(0)
    heads = cols // hd

    @pl.when(step == 0)
    def _():
        top_ref[...] = jnp.full(top_ref.shape, -1e30, jnp.float32)
        sum_ref[...] = jnp.zeros(sum_ref.shape, jnp.float32)
        acc_ref[...] = jnp.zeros(acc_ref.shape, jnp.float32)

    q = q_ref[...]
    lanes = lax.broadcasted_iota(jnp.int32, q.shape, 1)
    query = jnp.where(lanes < hd, q, jnp.zeros_like(q))
    group = GROUP if kv_ref.shape[0] % GROUP == 0 else 1
    for first in range(0, kv_ref.shape[0], group):
        scores, values = [], []
        for chunk in range(first, first + group):
            for part in range(tokens // sub):
                keys = kv_ref[chunk, part * sub : (part + 1) * sub, :]
                values.append(keys)
                live = kv_ref[chunk, tokens + part : tokens + part + 1, :sub]
                bias = jnp.where(live > 0, 0.0, -1e30).astype(jnp.float32)
                scores.append(
                    lax.dot_general(
                        query, keys, (((1,), (1,)), ((), ())), preferred_element_type=jnp.float32
                    )
                    * scale
                    + bias
                )
        top_old = top_ref[...]
        top_new = top_old
        for block in scores:
            top_new = jnp.maximum(top_new, jnp.max(block, axis=-1, keepdims=True))
        factor = jnp.exp(top_old - top_new)
        total = sum_ref[...] * factor
        accum = acc_ref[...] * factor
        for block, value in zip(scores, values):
            expo = jnp.exp(block - top_new)
            total = total + jnp.sum(expo, axis=-1, keepdims=True)
            accum = accum + jnp.dot(
                expo.astype(jnp.bfloat16), value, preferred_element_type=jnp.float32
            )
        sum_ref[...] = total
        acc_ref[...] = accum
        top_ref[...] = top_new

    @pl.when(step == pl.num_programs(0) - 1)
    def _():
        ratio = acc_ref[...] / sum_ref[...]
        o_ref[...] = ratio[:, hd:].astype(o_ref.dtype)


def attend(query, gathered, tokens, hd, scale, sub):
    parts, rows, span = gathered.shape
    qrows = query.shape[0]
    per = CHUNKS_PER_STEP if parts % CHUNKS_PER_STEP == 0 else 1
    kernel = lambda *refs: attend_kernel(
        *refs, tokens=tokens, cols=span, hd=hd, scale=scale, sub=sub
    )
    return pl.pallas_call(
        kernel,
        grid=(parts // per,),
        in_specs=[
            pl.BlockSpec(query.shape, lambda i: (0, 0)),
            pl.BlockSpec((per, rows, span), lambda i: (i, 0, 0)),
        ],
        out_specs=pl.BlockSpec((qrows, span - hd), lambda i: (0, 0)),
        out_shape=jax.ShapeDtypeStruct((qrows, span - hd), jnp.bfloat16),
        scratch_shapes=[
            pltpu.VMEM((qrows, 1), jnp.float32),
            pltpu.VMEM((qrows, 1), jnp.float32),
            pltpu.VMEM((qrows, span), jnp.float32),
        ],
    )(query, gathered)


def with_halo(cells, axis, width):
    count = lax.axis_size(axis[0]) * lax.axis_size(axis[1])
    ends = count - 1
    head = lax.slice_in_dim(cells, 0, width, axis=0)
    tail = lax.slice_in_dim(cells, cells.shape[0] - width, cells.shape[0], axis=0)
    return jnp.concatenate(
        [
            lax.ppermute(tail, axis, [(i, i + 1) for i in range(ends)]),
            cells,
            lax.ppermute(head, axis, [(i + 1, i) for i in range(ends)]),
        ],
        axis=0,
    )


def convolve(rimmed, weight):
    chans = weight.shape[1]
    kernel = weight.reshape(3, 3, 3, chans, weight.shape[2])
    out = lax.conv_general_dilated(
        rimmed[None],
        kernel,
        window_strides=(1, 1, 1),
        padding=((0, 0), (1, 1), (1, 1)),
        dimension_numbers=("NDHWC", "DHWIO", "NDHWC"),
        preferred_element_type=jnp.float32,
    )
    return out[0]


def to_cells(field):
    nx, ny, nz, count = field.shape
    blocks = field.reshape(nx // 2, 2, ny // 2, 2, nz // 2, 2, count).transpose(0, 2, 4, 1, 3, 5, 6)
    return blocks.reshape(nx // 2 * (ny // 2) * (nz // 2), 8 * count)


def body(
    features, mask, conv1_weight, conv2_weight, down_weight, norm_gain, qkv_weight, out_weight
):
    member = lax.axis_index("head")
    nx, ny, nz, local = features.shape
    width = down_weight.shape[2]
    chans = conv1_weight.shape[1]
    tokens = nx // 2 * (ny // 2) * (nz // 2)
    occupied = mask.astype(jnp.float32)[..., None]
    masked = features * mask.astype(jnp.bfloat16)[..., None]
    halo = with_halo(masked, SPACE, 1)
    rimmed = gather_head(lambda shift: halo)
    rimmed = jnp.moveaxis(rimmed, 0, 3).reshape(halo.shape[:3] + (-1,))
    whole_masked = lax.slice_in_dim(rimmed, 1, nx + 1, axis=0)
    pre1 = convolve(rimmed, conv1_weight)
    hidden = (occupied * jax.nn.silu(pre1)).astype(jnp.bfloat16)
    pre2 = convolve(with_halo(hidden, SPACE, 1), conv2_weight)
    refined_all = (occupied * (whole_masked.astype(jnp.float32) + pre2)).astype(jnp.bfloat16)
    refined = lax.dynamic_slice_in_dim(refined_all, member * local, local, 3)
    coarse = jnp.dot(
        to_cells(refined_all),
        down_weight.reshape(8 * chans, width),
        preferred_element_type=jnp.float32,
    ).astype(jnp.bfloat16)
    wide = coarse.astype(jnp.float32)
    normed = (
        wide * lax.rsqrt(jnp.mean(wide * wide, axis=1, keepdims=True) + 1e-05) * norm_gain
    ).astype(jnp.bfloat16)
    local_cols = qkv_weight.shape[2]
    proj = jnp.dot(
        normed, qkv_weight.reshape(width, 3 * local_cols), preferred_element_type=jnp.float32
    )
    proj = proj.astype(jnp.bfloat16).reshape(tokens, 3, local_cols)
    head_size = width // HEADS
    heads_here = local_cols // head_size
    query = proj[:, 0]
    live_cell = (
        mask.reshape(nx // 2, 2, ny // 2, 2, nz // 2, 2)
        .max(axis=(1, 3, 5))
        .reshape(1, -1)
        .astype(jnp.bfloat16)
    )
    core = lax.axis_index("core")
    swap = [(0, 1), (1, 0)]
    qkv = proj.reshape(tokens, 3, heads_here, head_size)
    keep = lax.dynamic_index_in_dim(qkv, core, 2, keepdims=False)
    send = lax.dynamic_index_in_dim(qkv, 1 - core, 2, keepdims=False)
    both = jnp.concatenate([send.reshape(tokens, 3 * head_size), live_cell.reshape(tokens, 1).astype(jnp.bfloat16)], 1)
    got = lax.ppermute(both, "core", swap)
    mine = jnp.concatenate([keep.reshape(tokens, 3 * head_size), live_cell.reshape(tokens, 1).astype(jnp.bfloat16)], 1)
    chip = jnp.where(core == 0, jnp.concatenate([mine, got], 0), jnp.concatenate([got, mine], 0))
    chip_tokens = 2 * tokens
    sub = 2 * head_size
    query = jnp.pad(chip[:, :head_size], ((0, 0), (0, head_size)))
    live_rows = chip[:, 3 * head_size].reshape(chip_tokens // sub, sub)
    live_rows = jnp.pad(live_rows, ((0, (-live_rows.shape[0]) % 16), (0, 0)))
    piece = jnp.concatenate([chip[:, head_size : 3 * head_size], live_rows], axis=0)
    gathered = lax.all_gather(piece[None], "chip", axis=0, tiled=True)
    scale = head_size ** (-0.5)
    half = attend(query, gathered, chip_tokens, head_size, scale, sub)
    own = lax.dynamic_slice_in_dim(half, core * tokens, tokens, 0)
    other = lax.ppermute(lax.dynamic_slice_in_dim(half, (1 - core) * tokens, tokens, 0), "core", swap)
    attn = jnp.where(core == 0, jnp.concatenate([own, other], 1), jnp.concatenate([other, own], 1))
    cols_w = gather_head(
        lambda shift: lax.dynamic_slice_in_dim(
            out_weight, (member + shift) % lax.axis_size("head") * local_cols, local_cols, 1
        )
    ).reshape(width, local_cols)
    attn_all = jnp.moveaxis(gather_head(lambda shift: attn), 0, 1).reshape(tokens, width)
    mixed = jnp.dot(attn_all, cols_w, preferred_element_type=jnp.float32)
    mine = lax.dynamic_slice_in_dim(wide, member * local_cols, local_cols, 1)
    level_out = (mine + mixed).astype(jnp.bfloat16)
    return (refined, level_out)


def solution(mesh):
    space = mesh.shape["space"]
    devices = mesh.devices.reshape(space // 2, 2, mesh.shape["head"])
    split = jax.sharding.Mesh(devices, ("chip", "core", "head"))
    in_specs = (
        P(SPACE, None, None, "head"),
        P(SPACE, None, None),
        P(),
        P(),
        P(),
        P(),
        P(None, None, "head"),
        P("head", None),
    )
    out_specs = (P(SPACE, None, None, "head"), P(SPACE, "head"))
    return jax.shard_map(body, mesh=split, in_specs=in_specs, out_specs=out_specs, check_vma=False)
```

```python
import jax
import jax.numpy as jnp
from jax import lax
from jax.experimental import pallas as pl
from jax.experimental.pallas import tpu as pltpu
from jax.sharding import PartitionSpec as P

HEADS = 8
SPACE = ("chip", "core")
CHUNKS_PER_STEP = 8
GROUP = 4


def gather_head(piece_for):
    count = lax.axis_size("head")
    member = lax.axis_index("head")
    got = [piece_for(0)]
    for shift in range(1, count):
        got.append(
            lax.ppermute(
                piece_for(shift), "head", [(i, (i + shift) % count) for i in range(count)]
            )
        )
    ring = jnp.stack([got[0]] + [got[count - t] for t in range(1, count)])
    twice = jnp.concatenate([ring, ring], axis=0)
    return lax.dynamic_slice_in_dim(twice, (count - member) % count, count, axis=0)


def attend_kernel(q_ref, kv_ref, o_ref, top_ref, sum_ref, acc_ref, *, tokens, cols, hd, scale, sub):
    step = pl.program_id(0)
    heads = cols // hd

    @pl.when(step == 0)
    def _():
        top_ref[...] = jnp.full(top_ref.shape, -1e30, jnp.float32)
        sum_ref[...] = jnp.zeros(sum_ref.shape, jnp.float32)
        acc_ref[...] = jnp.zeros(acc_ref.shape, jnp.float32)

    q = q_ref[...]
    lanes = lax.broadcasted_iota(jnp.int32, q.shape, 1)
    query = jnp.where(lanes < hd, q, jnp.zeros_like(q))
    group = GROUP if kv_ref.shape[0] % GROUP == 0 else 1
    for first in range(0, kv_ref.shape[0], group):
        scores, values = [], []
        for chunk in range(first, first + group):
            for part in range(tokens // sub):
                keys = kv_ref[chunk, part * sub : (part + 1) * sub, :]
                values.append(keys)
                live = kv_ref[chunk, tokens + part : tokens + part + 1, :sub]
                bias = jnp.where(live > 0, 0.0, -1e30).astype(jnp.float32)
                scores.append(
                    lax.dot_general(
                        query, keys, (((1,), (1,)), ((), ())), preferred_element_type=jnp.float32
                    )
                    * scale
                    + bias
                )
        top_old = top_ref[...]
        top_new = top_old
        for block in scores:
            top_new = jnp.maximum(top_new, jnp.max(block, axis=-1, keepdims=True))
        factor = jnp.exp(top_old - top_new)
        total = sum_ref[...] * factor
        accum = acc_ref[...] * factor
        for block, value in zip(scores, values):
            expo = jnp.exp(block - top_new)
            total = total + jnp.sum(expo, axis=-1, keepdims=True)
            accum = accum + jnp.dot(
                expo.astype(jnp.bfloat16), value, preferred_element_type=jnp.float32
            )
        sum_ref[...] = total
        acc_ref[...] = accum
        top_ref[...] = top_new

    @pl.when(step == pl.num_programs(0) - 1)
    def _():
        ratio = acc_ref[...] / sum_ref[...]
        o_ref[...] = ratio[:, hd:].astype(o_ref.dtype)


def attend(query, gathered, tokens, hd, scale, sub):
    parts, rows, span = gathered.shape
    qrows = query.shape[0]
    per = CHUNKS_PER_STEP if parts % CHUNKS_PER_STEP == 0 else 1
    kernel = lambda *refs: attend_kernel(
        *refs, tokens=tokens, cols=span, hd=hd, scale=scale, sub=sub
    )
    return pl.pallas_call(
        kernel,
        grid=(parts // per,),
        in_specs=[
            pl.BlockSpec(query.shape, lambda i: (0, 0)),
            pl.BlockSpec((per, rows, span), lambda i: (i, 0, 0)),
        ],
        out_specs=pl.BlockSpec((qrows, span - hd), lambda i: (0, 0)),
        out_shape=jax.ShapeDtypeStruct((qrows, span - hd), jnp.bfloat16),
        scratch_shapes=[
            pltpu.VMEM((qrows, 1), jnp.float32),
            pltpu.VMEM((qrows, 1), jnp.float32),
            pltpu.VMEM((qrows, span), jnp.float32),
        ],
    )(query, gathered)


def with_halo(cells, axis, width):
    count = lax.axis_size(axis[0]) * lax.axis_size(axis[1])
    ends = count - 1
    head = lax.slice_in_dim(cells, 0, width, axis=0)
    tail = lax.slice_in_dim(cells, cells.shape[0] - width, cells.shape[0], axis=0)
    return jnp.concatenate(
        [
            lax.ppermute(tail, axis, [(i, i + 1) for i in range(ends)]),
            cells,
            lax.ppermute(head, axis, [(i + 1, i) for i in range(ends)]),
        ],
        axis=0,
    )


def convolve(rimmed, weight):
    chans = weight.shape[1]
    kernel = weight.reshape(3, 3, 3, chans, weight.shape[2])
    out = lax.conv_general_dilated(
        rimmed[None],
        kernel,
        window_strides=(1, 1, 1),
        padding=((0, 0), (1, 1), (1, 1)),
        dimension_numbers=("NDHWC", "DHWIO", "NDHWC"),
        preferred_element_type=jnp.float32,
    )
    return out[0]


def to_cells(field):
    nx, ny, nz, count = field.shape
    blocks = field.reshape(nx // 2, 2, ny // 2, 2, nz // 2, 2, count).transpose(0, 2, 4, 1, 3, 5, 6)
    return blocks.reshape(nx // 2 * (ny // 2) * (nz // 2), 8 * count)


def body(
    features, mask, conv1_weight, conv2_weight, down_weight, norm_gain, qkv_weight, out_weight
):
    member = lax.axis_index("head")
    nx, ny, nz, local = features.shape
    width = down_weight.shape[2]
    chans = conv1_weight.shape[1]
    tokens = nx // 2 * (ny // 2) * (nz // 2)
    occupied = mask.astype(jnp.float32)[..., None]
    masked = features * mask.astype(jnp.bfloat16)[..., None]
    whole = gather_head(lambda shift: features)
    whole = jnp.moveaxis(whole, 0, 3).reshape(features.shape[:3] + (-1,))
    whole_masked = whole * mask.astype(jnp.bfloat16)[..., None]
    rimmed = with_halo(whole_masked, SPACE, 1)
    pre1 = convolve(rimmed, conv1_weight)
    hidden = (occupied * jax.nn.silu(pre1)).astype(jnp.bfloat16)
    pre2 = convolve(with_halo(hidden, SPACE, 1), conv2_weight)
    refined_all = (occupied * (whole_masked.astype(jnp.float32) + pre2)).astype(jnp.bfloat16)
    refined = lax.dynamic_slice_in_dim(refined_all, member * local, local, 3)
    coarse = jnp.dot(
        to_cells(refined_all),
        down_weight.reshape(8 * chans, width),
        preferred_element_type=jnp.float32,
    ).astype(jnp.bfloat16)
    wide = coarse.astype(jnp.float32)
    normed = (
        wide * lax.rsqrt(jnp.mean(wide * wide, axis=1, keepdims=True) + 1e-05) * norm_gain
    ).astype(jnp.bfloat16)
    local_cols = qkv_weight.shape[2]
    proj = jnp.dot(
        normed, qkv_weight.reshape(width, 3 * local_cols), preferred_element_type=jnp.float32
    )
    proj = proj.astype(jnp.bfloat16).reshape(tokens, 3, local_cols)
    head_size = width // HEADS
    heads_here = local_cols // head_size
    query = proj[:, 0]
    live_cell = (
        mask.reshape(nx // 2, 2, ny // 2, 2, nz // 2, 2)
        .max(axis=(1, 3, 5))
        .reshape(1, -1)
        .astype(jnp.bfloat16)
    )
    core = lax.axis_index("core")
    swap = [(0, 1), (1, 0)]
    qkv = proj.reshape(tokens, 3, heads_here, head_size)
    keep = lax.dynamic_index_in_dim(qkv, core, 2, keepdims=False)
    send = lax.dynamic_index_in_dim(qkv, 1 - core, 2, keepdims=False)
    both = jnp.concatenate([send.reshape(tokens, 3 * head_size), live_cell.reshape(tokens, 1).astype(jnp.bfloat16)], 1)
    got = lax.ppermute(both, "core", swap)
    mine = jnp.concatenate([keep.reshape(tokens, 3 * head_size), live_cell.reshape(tokens, 1).astype(jnp.bfloat16)], 1)
    chip = jnp.where(core == 0, jnp.concatenate([mine, got], 0), jnp.concatenate([got, mine], 0))
    chip_tokens = 2 * tokens
    sub = 2 * head_size
    query = jnp.pad(chip[:, :head_size], ((0, 0), (0, head_size)))
    live_rows = chip[:, 3 * head_size].reshape(chip_tokens // sub, sub)
    live_rows = jnp.pad(live_rows, ((0, (-live_rows.shape[0]) % 16), (0, 0)))
    piece = jnp.concatenate([chip[:, head_size : 3 * head_size], live_rows], axis=0)
    gathered = lax.all_gather(piece[None], "chip", axis=0, tiled=True)
    scale = head_size ** (-0.5)
    half = attend(query, gathered, chip_tokens, head_size, scale, sub)
    own = lax.dynamic_slice_in_dim(half, core * tokens, tokens, 0)
    other = lax.ppermute(lax.dynamic_slice_in_dim(half, (1 - core) * tokens, tokens, 0), "core", swap)
    attn = jnp.where(core == 0, jnp.concatenate([own, other], 1), jnp.concatenate([other, own], 1))
    cols_w = gather_head(
        lambda shift: lax.dynamic_slice_in_dim(
            out_weight, (member + shift) % lax.axis_size("head") * local_cols, local_cols, 1
        )
    ).reshape(width, local_cols)
    attn_all = jnp.moveaxis(gather_head(lambda shift: attn), 0, 1).reshape(tokens, width)
    mixed = jnp.dot(attn_all, cols_w, preferred_element_type=jnp.float32)
    mine = lax.dynamic_slice_in_dim(wide, member * local_cols, local_cols, 1)
    level_out = (mine + mixed).astype(jnp.bfloat16)
    return (refined, level_out)


def solution(mesh):
    space = mesh.shape["space"]
    devices = mesh.devices.reshape(space // 2, 2, mesh.shape["head"])
    split = jax.sharding.Mesh(devices, ("chip", "core", "head"))
    in_specs = (
        P(SPACE, None, None, "head"),
        P(SPACE, None, None),
        P(),
        P(),
        P(),
        P(),
        P(None, None, "head"),
        P("head", None),
    )
    out_specs = (P(SPACE, None, None, "head"), P(SPACE, "head"))
    return jax.shard_map(body, mesh=split, in_specs=in_specs, out_specs=out_specs, check_vma=False)
```

```python
import jax
import jax.numpy as jnp
from jax import lax
from jax.experimental import pallas as pl
from jax.experimental.pallas import tpu as pltpu
from jax.sharding import PartitionSpec as P

HEADS = 8
SPACE = ("chip", "core")
CHUNKS_PER_STEP = 8
GROUP = 8


def gather_head(piece_for):
    count = lax.axis_size("head")
    member = lax.axis_index("head")
    got = [piece_for(0)]
    for shift in range(1, count):
        got.append(
            lax.ppermute(
                piece_for(shift), "head", [(i, (i + shift) % count) for i in range(count)]
            )
        )
    ring = jnp.stack([got[0]] + [got[count - t] for t in range(1, count)])
    twice = jnp.concatenate([ring, ring], axis=0)
    return lax.dynamic_slice_in_dim(twice, (count - member) % count, count, axis=0)


def attend_kernel(q_ref, kv_ref, o_ref, top_ref, sum_ref, acc_ref, *, tokens, cols, hd, scale, sub):
    step = pl.program_id(0)
    heads = cols // hd

    @pl.when(step == 0)
    def _():
        top_ref[...] = jnp.full(top_ref.shape, -1e30, jnp.float32)
        sum_ref[...] = jnp.zeros(sum_ref.shape, jnp.float32)
        acc_ref[...] = jnp.zeros(acc_ref.shape, jnp.float32)

    q = q_ref[...]
    lanes = lax.broadcasted_iota(jnp.int32, q.shape, 1)
    query = jnp.where(lanes < hd, q, jnp.zeros_like(q))
    group = GROUP if kv_ref.shape[0] % GROUP == 0 else 1
    for first in range(0, kv_ref.shape[0], group):
        scores, values = [], []
        for chunk in range(first, first + group):
            for part in range(tokens // sub):
                keys = kv_ref[chunk, part * sub : (part + 1) * sub, :]
                values.append(keys)
                live = kv_ref[chunk, tokens + part : tokens + part + 1, :sub]
                bias = jnp.where(live > 0, 0.0, -1e30).astype(jnp.float32)
                scores.append(
                    lax.dot_general(
                        query, keys, (((1,), (1,)), ((), ())), preferred_element_type=jnp.float32
                    )
                    * scale
                    + bias
                )
        top_old = top_ref[...]
        top_new = top_old
        for block in scores:
            top_new = jnp.maximum(top_new, jnp.max(block, axis=-1, keepdims=True))
        factor = jnp.exp(top_old - top_new)
        total = sum_ref[...] * factor
        accum = acc_ref[...] * factor
        for block, value in zip(scores, values):
            expo = jnp.exp(block - top_new)
            total = total + jnp.sum(expo, axis=-1, keepdims=True)
            accum = accum + jnp.dot(
                expo.astype(jnp.bfloat16), value, preferred_element_type=jnp.float32
            )
        sum_ref[...] = total
        acc_ref[...] = accum
        top_ref[...] = top_new

    @pl.when(step == pl.num_programs(0) - 1)
    def _():
        ratio = acc_ref[...] / sum_ref[...]
        o_ref[...] = ratio[:, hd:].astype(o_ref.dtype)


def attend(query, gathered, tokens, hd, scale, sub):
    parts, rows, span = gathered.shape
    qrows = query.shape[0]
    per = CHUNKS_PER_STEP if parts % CHUNKS_PER_STEP == 0 else 1
    kernel = lambda *refs: attend_kernel(
        *refs, tokens=tokens, cols=span, hd=hd, scale=scale, sub=sub
    )
    return pl.pallas_call(
        kernel,
        grid=(parts // per,),
        in_specs=[
            pl.BlockSpec(query.shape, lambda i: (0, 0)),
            pl.BlockSpec((per, rows, span), lambda i: (i, 0, 0)),
        ],
        out_specs=pl.BlockSpec((qrows, span - hd), lambda i: (0, 0)),
        out_shape=jax.ShapeDtypeStruct((qrows, span - hd), jnp.bfloat16),
        scratch_shapes=[
            pltpu.VMEM((qrows, 1), jnp.float32),
            pltpu.VMEM((qrows, 1), jnp.float32),
            pltpu.VMEM((qrows, span), jnp.float32),
        ],
    )(query, gathered)


def with_halo(cells, axis, width):
    count = lax.axis_size(axis[0]) * lax.axis_size(axis[1])
    ends = count - 1
    head = lax.slice_in_dim(cells, 0, width, axis=0)
    tail = lax.slice_in_dim(cells, cells.shape[0] - width, cells.shape[0], axis=0)
    return jnp.concatenate(
        [
            lax.ppermute(tail, axis, [(i, i + 1) for i in range(ends)]),
            cells,
            lax.ppermute(head, axis, [(i + 1, i) for i in range(ends)]),
        ],
        axis=0,
    )


def convolve(rimmed, weight):
    chans = weight.shape[1]
    kernel = weight.reshape(3, 3, 3, chans, weight.shape[2])
    out = lax.conv_general_dilated(
        rimmed[None],
        kernel,
        window_strides=(1, 1, 1),
        padding=((0, 0), (1, 1), (1, 1)),
        dimension_numbers=("NDHWC", "DHWIO", "NDHWC"),
        preferred_element_type=jnp.float32,
    )
    return out[0]


def to_cells(field):
    nx, ny, nz, count = field.shape
    blocks = field.reshape(nx // 2, 2, ny // 2, 2, nz // 2, 2, count).transpose(0, 2, 4, 1, 3, 5, 6)
    return blocks.reshape(nx // 2 * (ny // 2) * (nz // 2), 8 * count)


def body(
    features, mask, conv1_weight, conv2_weight, down_weight, norm_gain, qkv_weight, out_weight
):
    member = lax.axis_index("head")
    nx, ny, nz, local = features.shape
    width = down_weight.shape[2]
    chans = conv1_weight.shape[1]
    tokens = nx // 2 * (ny // 2) * (nz // 2)
    occupied = mask.astype(jnp.float32)[..., None]
    masked = features * mask.astype(jnp.bfloat16)[..., None]
    whole = gather_head(lambda shift: features)
    whole = jnp.moveaxis(whole, 0, 3).reshape(features.shape[:3] + (-1,))
    whole_masked = whole * mask.astype(jnp.bfloat16)[..., None]
    rimmed = with_halo(whole_masked, SPACE, 1)
    pre1 = convolve(rimmed, conv1_weight)
    hidden = (occupied * jax.nn.silu(pre1)).astype(jnp.bfloat16)
    pre2 = convolve(with_halo(hidden, SPACE, 1), conv2_weight)
    refined_all = (occupied * (whole_masked.astype(jnp.float32) + pre2)).astype(jnp.bfloat16)
    refined = lax.dynamic_slice_in_dim(refined_all, member * local, local, 3)
    coarse = jnp.dot(
        to_cells(refined_all),
        down_weight.reshape(8 * chans, width),
        preferred_element_type=jnp.float32,
    ).astype(jnp.bfloat16)
    wide = coarse.astype(jnp.float32)
    normed = (
        wide * lax.rsqrt(jnp.mean(wide * wide, axis=1, keepdims=True) + 1e-05) * norm_gain
    ).astype(jnp.bfloat16)
    local_cols = qkv_weight.shape[2]
    proj = jnp.dot(
        normed, qkv_weight.reshape(width, 3 * local_cols), preferred_element_type=jnp.float32
    )
    proj = proj.astype(jnp.bfloat16).reshape(tokens, 3, local_cols)
    head_size = width // HEADS
    heads_here = local_cols // head_size
    query = proj[:, 0]
    live_cell = (
        mask.reshape(nx // 2, 2, ny // 2, 2, nz // 2, 2)
        .max(axis=(1, 3, 5))
        .reshape(1, -1)
        .astype(jnp.bfloat16)
    )
    core = lax.axis_index("core")
    swap = [(0, 1), (1, 0)]
    qkv = proj.reshape(tokens, 3, heads_here, head_size)
    keep = lax.dynamic_index_in_dim(qkv, core, 2, keepdims=False)
    send = lax.dynamic_index_in_dim(qkv, 1 - core, 2, keepdims=False)
    both = jnp.concatenate([send.reshape(tokens, 3 * head_size), live_cell.reshape(tokens, 1).astype(jnp.bfloat16)], 1)
    got = lax.ppermute(both, "core", swap)
    mine = jnp.concatenate([keep.reshape(tokens, 3 * head_size), live_cell.reshape(tokens, 1).astype(jnp.bfloat16)], 1)
    chip = jnp.where(core == 0, jnp.concatenate([mine, got], 0), jnp.concatenate([got, mine], 0))
    chip_tokens = 2 * tokens
    sub = 2 * head_size
    query = jnp.pad(chip[:, :head_size], ((0, 0), (0, head_size)))
    live_rows = chip[:, 3 * head_size].reshape(chip_tokens // sub, sub)
    live_rows = jnp.pad(live_rows, ((0, (-live_rows.shape[0]) % 16), (0, 0)))
    piece = jnp.concatenate([chip[:, head_size : 3 * head_size], live_rows], axis=0)
    gathered = lax.all_gather(piece[None], "chip", axis=0, tiled=True)
    scale = head_size ** (-0.5)
    half = attend(query, gathered, chip_tokens, head_size, scale, sub)
    own = lax.dynamic_slice_in_dim(half, core * tokens, tokens, 0)
    other = lax.ppermute(lax.dynamic_slice_in_dim(half, (1 - core) * tokens, tokens, 0), "core", swap)
    attn = jnp.where(core == 0, jnp.concatenate([own, other], 1), jnp.concatenate([other, own], 1))
    cols_w = gather_head(
        lambda shift: lax.dynamic_slice_in_dim(
            out_weight, (member + shift) % lax.axis_size("head") * local_cols, local_cols, 1
        )
    ).reshape(width, local_cols)
    attn_all = jnp.moveaxis(gather_head(lambda shift: attn), 0, 1).reshape(tokens, width)
    mixed = jnp.dot(attn_all, cols_w, preferred_element_type=jnp.float32)
    mine = lax.dynamic_slice_in_dim(wide, member * local_cols, local_cols, 1)
    level_out = (mine + mixed).astype(jnp.bfloat16)
    return (refined, level_out)


def solution(mesh):
    space = mesh.shape["space"]
    devices = mesh.devices.reshape(space // 2, 2, mesh.shape["head"])
    split = jax.sharding.Mesh(devices, ("chip", "core", "head"))
    in_specs = (
        P(SPACE, None, None, "head"),
        P(SPACE, None, None),
        P(),
        P(),
        P(),
        P(),
        P(None, None, "head"),
        P("head", None),
    )
    out_specs = (P(SPACE, None, None, "head"), P(SPACE, "head"))
    return jax.shard_map(body, mesh=split, in_specs=in_specs, out_specs=out_specs, check_vma=False)
```
